512 devices in a mesh: req: 128 (over y, z, core), tp: 4 (over x).
Axes of the slice: x: 4, y: 8, z: 8, core: 2. Of those that a mesh axis runs over, the one named last changes fastest.
Arguments:
- tokens: bfloat16 [65536, 1024], P('req', 'tp')
- placement: int32 [16384], P('req'), may hold values from 0 to 16383, as said below
- cache_len: int32 [256], P('req'), may hold values from 0 to 1024, as said below
- w_query: bfloat16 [1024, 1024], P(None, 'tp'), may hold values from -0.1875 to 0.1875
- w_key: bfloat16 [1024, 1024], P(None, 'tp'), may hold values from -0.1875 to 0.1875
- w_value: bfloat16 [1024, 1024], P(None, 'tp'), may hold values from -0.1875 to 0.1875
- w_out: bfloat16 [1024, 1024], P('tp'), may hold values from -0.1875 to 0.1875
- k_cache: bfloat16 [256, 1024, 1024], P('req', None, 'tp'), may hold values from -6 to 6
- v_cache: bfloat16 [256, 1024, 1024], P('req', None, 'tp'), may hold values from -6 to 6
- ln_gain: float32 [1024], replicated, may hold values from 0.1 to 1.9
- ln_bias: float32 [1024], replicated, may hold values from -0.5 to 0.5
Outputs:
- mixed: bfloat16 [65536, 1024], P('req', 'tp')
The draws below stay inside these ranges and needn't reach their ends.
Inputs may be any that keep to these rules, and one draw needn't show every extreme that they name: `placement`: A permutation of the blocks. Of the 128 blocks that arrive on index s of req, exactly one goes to the owner range of every index t of req, and it lands at owner position t * 128 + s. `cache_len`: some request has exactly 1024 cached positions.
All inputs are finite; a program needn't handle non-finite values.
Results may differ from the reference program's by a relative error of at most 0.014.
The reference program's roundings to bfloat16 on the way (of `owned`, `queries`, `weight_low`, `context` and `normed`) count: a program that leaves them out, or rounds other values in their place, can miss the bound.
Values may be sent and summed in bfloat16 or wider, within the bound.
No kernel may reach another device: no remote copies, remote signals or barrier semaphores. Data moves between devices by JAX's collectives and lax.ppermute only.
A program may use at most 64 MiB of HBM per device.

```python
import jax
import jax.numpy as jnp
from jax import lax

D = 1024
HEADS = 16
BLOCKS_DEV = 128
BLOCK_ROWS = 4
PREFILL_LEN = 256
CACHE_MAX = 1024
REQUESTS = 256
BLOCKS = 16384
ROWS = 65536
N_REQ = 128


def draw_tokens(key, part):
    base = jnp.clip(jax.random.normal(key, (ROWS, D), jnp.float32), -6.0, 6.0)
    return base.astype(jnp.bfloat16)


def draw_placement(key, part):
    per_peer = BLOCKS_DEV // N_REQ
    keys = jax.random.split(key, N_REQ)
    local = jax.vmap(lambda one_key: jax.random.permutation(one_key, BLOCKS_DEV))(keys).astype(jnp.int32)
    source = jnp.arange(N_REQ, dtype=jnp.int32)[:, None]
    owner_dev = local // per_peer
    offset = local % per_peer
    return (owner_dev * BLOCKS_DEV + source * per_peer + offset).reshape(BLOCKS).astype(jnp.int32)


def draw_cache_len(key, part):
    lengths = jax.random.randint(key, (REQUESTS,), 0, CACHE_MAX + 1, dtype=jnp.int32)
    chosen = jax.random.randint(jax.random.fold_in(key, 3), (), 0, REQUESTS, dtype=jnp.int32)
    return lengths.at[chosen].set(CACHE_MAX).astype(jnp.int32)


def block_scale(stream_key, extent, cuts, smallest, top_value):
    def one(axis_at, shards_of):
        draws = jax.random.uniform(jax.random.fold_in(jax.random.fold_in(stream_key, 6), axis_at), (shards_of,), jnp.float32, smallest / len(cuts), top_value / len(cuts))
        return jnp.repeat(jnp.exp(draws), extent[axis_at] // shards_of).reshape((-1,) + (1,) * (len(extent) - axis_at - 1))

    loudness = one(*cuts[0])
    for cut in cuts[1:]:
        loudness = loudness * one(*cut)
    return loudness


def normal_values(stream_key, extent, scale, most, cuts=(), kind=jnp.bfloat16):
    entries = jax.random.normal(stream_key, extent, jnp.float32) * scale
    if len(cuts) > 0:
        entries = block_scale(stream_key, extent, cuts, -0.22, 0.18) * entries
    return jnp.clip(entries, min=-most, max=most).astype(kind)


def setup_inputs(seed: int = 0) -> dict:
    splits = jax.random.split(jax.random.key(seed), 12)
    tokens = draw_tokens(jax.random.fold_in(splits[11], 71), 0)
    placement = draw_placement(jax.random.fold_in(splits[11], 71), 0)
    cache_len = draw_cache_len(jax.random.fold_in(splits[11], 71), 0)
    w_query = normal_values(splits[3], (D, D), D ** -0.5, 0.1875, ((1, 4),))
    w_key = normal_values(splits[4], (D, D), D ** -0.5, 0.1875, ((1, 4),))
    w_value = normal_values(splits[5], (D, D), D ** -0.5, 0.1875, ((1, 4),))
    w_out = normal_values(splits[6], (D, D), D ** -0.5, 0.1875, ((0, 4),))
    k_cache = normal_values(splits[7], (REQUESTS, CACHE_MAX, D), 1.0, 6.0, ((0, 128), (2, 4)))
    v_cache = normal_values(splits[8], (REQUESTS, CACHE_MAX, D), 1.0, 6.0, ((0, 128), (2, 4)))
    ln_gain = jnp.clip(1.0 + 0.18 * jax.random.normal(splits[9], (D,), jnp.float32), 0.1, 1.9)
    ln_bias = jnp.clip(jax.random.uniform(splits[10], (D,), jnp.float32, -0.5, 0.5), -0.5, 0.5)
    return {"tokens": tokens, "placement": placement, "cache_len": cache_len, "w_query": w_query, "w_key": w_key, "w_value": w_value, "w_out": w_out, "k_cache": k_cache, "v_cache": v_cache, "ln_gain": ln_gain, "ln_bias": ln_bias}


def attend_request(queries, new_keys, new_values, cache_keys, cache_values, length):
    head_size = D // HEADS
    new_count = queries.shape[0]
    span = cache_keys.shape[0]
    keys_all = jnp.concatenate([cache_keys, new_keys], 0).reshape(span + new_count, HEADS, head_size).astype(jnp.float32)
    values_all = jnp.concatenate([cache_values, new_values], 0).reshape(span + new_count, HEADS, head_size).astype(jnp.float32)
    query_heads = queries.reshape(new_count, HEADS, head_size).astype(jnp.float32)
    scores = jnp.einsum('qhd,khd->hqk', query_heads, keys_all) * head_size ** (-0.5)
    key_pos = jnp.arange(span + new_count, dtype=jnp.int32)[None, :]
    query_pos = jnp.arange(new_count, dtype=jnp.int32)[:, None]
    valid = jnp.where(key_pos < span, key_pos < length, key_pos - span <= query_pos)
    scores = jnp.where(valid[None], scores, -jnp.inf)
    top = lax.optimization_barrier(jnp.max(scores, axis=-1, keepdims=True))
    weight = jnp.where(valid[None], jnp.exp(scores - top), 0.0)
    total = lax.optimization_barrier(jnp.sum(weight, axis=-1))
    weight_low = weight.astype(jnp.bfloat16).astype(jnp.float32)
    context = jnp.einsum('hqk,khd->qhd', weight_low, values_all) / jnp.transpose(total)[:, :, None]
    return context.reshape(new_count, D).astype(jnp.bfloat16)

def reference(tokens, placement, cache_len, w_query, w_key, w_value, w_out, k_cache, v_cache, ln_gain, ln_bias):
    arrival = tokens.reshape(BLOCKS, BLOCK_ROWS, D)
    owned = jnp.zeros_like(arrival).at[placement].set(arrival).reshape(ROWS, D)
    queries = jnp.dot(owned, w_query, preferred_element_type=jnp.float32).astype(jnp.bfloat16)
    new_keys = jnp.dot(owned, w_key, preferred_element_type=jnp.float32).astype(jnp.bfloat16)
    new_values = jnp.dot(owned, w_value, preferred_element_type=jnp.float32).astype(jnp.bfloat16)
    shape_req = (REQUESTS, PREFILL_LEN, D)
    context = lax.map(lambda items: attend_request(*items), (queries.reshape(shape_req), new_keys.reshape(shape_req), new_values.reshape(shape_req), k_cache, v_cache, cache_len))
    context = context.reshape(ROWS, D)
    attended = jnp.dot(context, w_out, preferred_element_type=jnp.float32)
    summed = owned.astype(jnp.float32) + attended
    row_mean = lax.optimization_barrier(jnp.mean(summed, axis=1, keepdims=True))
    centered = summed - row_mean
    row_var = lax.optimization_barrier(jnp.mean(centered * centered, axis=1, keepdims=True))
    normed = (centered / jnp.sqrt(row_var + 1e-05) * ln_gain + ln_bias).astype(jnp.bfloat16)
    mixed = normed.reshape(BLOCKS, BLOCK_ROWS, D)[placement].reshape(ROWS, D)
    return mixed
```

```python
import jax
import jax.numpy as jnp
from jax import lax
from jax.sharding import PartitionSpec as P

D = 1024
HEADS = 16


def gather_tp(part):
    count = lax.axis_size("tp")
    copies = jnp.broadcast_to(part[None], (count,) + part.shape)
    got = lax.all_to_all(copies, "tp", 0, 0, tiled=True)
    return jnp.moveaxis(got, 0, 1).reshape(part.shape[0], count * part.shape[1])


def scatter_sum_tp(whole):
    count = lax.axis_size("tp")
    rows, width = whole.shape
    pieces = jnp.moveaxis(whole.reshape(rows, count, width // count), 1, 0)
    got = lax.all_to_all(pieces, "tp", 0, 0, tiled=True)
    return jnp.sum(got.astype(jnp.float32), axis=0)


def sum_tp(stats):
    count = lax.axis_size("tp")
    copies = jnp.broadcast_to(stats[None], (count,) + stats.shape)
    got = lax.all_to_all(copies, "tp", 0, 0, tiled=True)
    return jnp.sum(got, axis=0)


def head_view(array, head_size):
    return array.reshape(array.shape[0], array.shape[1] // head_size, head_size)


def attend_padded(queries, new_keys, new_values, cache_keys, cache_values, length):
    head_size = D // HEADS
    new_count = queries.shape[0]
    span = cache_keys.shape[0]
    keys_all = head_view(jnp.concatenate([cache_keys, new_keys], 0), head_size)
    values_all = head_view(jnp.concatenate([cache_values, new_values], 0), head_size)
    query_heads = head_view(queries, head_size)
    scores = jnp.einsum(
        "qhd,khd->hqk", query_heads, keys_all, preferred_element_type=jnp.float32
    ) * head_size ** (-0.5)
    key_pos = jnp.arange(span + new_count, dtype=jnp.int32)[None, :]
    query_pos = jnp.arange(new_count, dtype=jnp.int32)[:, None]
    valid = jnp.where(key_pos < span, key_pos < length, key_pos - span <= query_pos)
    scores = jnp.where(valid[None], scores, -jnp.inf)
    top = jnp.max(scores, axis=-1, keepdims=True)
    weight = jnp.where(valid[None], jnp.exp(scores - top), 0.0)
    total = jnp.sum(weight, axis=-1)
    context = jnp.einsum(
        "hqk,khd->qhd", weight.astype(jnp.bfloat16), values_all, preferred_element_type=jnp.float32
    )
    context = context / jnp.transpose(total)[:, :, None]
    return context.reshape(new_count, queries.shape[1]).astype(jnp.bfloat16)


def attend_all(queries, new_keys, new_values, k_cache, v_cache, cache_len):
    request_count = k_cache.shape[0]
    req_shape = (request_count, queries.shape[0] // request_count, queries.shape[1])
    context = lax.map(
        lambda items: attend_padded(*items),
        (
            queries.reshape(req_shape),
            new_keys.reshape(req_shape),
            new_values.reshape(req_shape),
            k_cache,
            v_cache,
            cache_len,
        ),
    )
    return context.reshape(queries.shape)


def project_rows(whole, w_query, w_key, w_value):
    queries = jnp.dot(whole, w_query, preferred_element_type=jnp.float32).astype(jnp.bfloat16)
    new_keys = jnp.dot(whole, w_key, preferred_element_type=jnp.float32).astype(jnp.bfloat16)
    new_values = jnp.dot(whole, w_value, preferred_element_type=jnp.float32).astype(jnp.bfloat16)
    return (queries, new_keys, new_values)


def finish_rows(context, local, w_out, ln_gain, ln_bias):
    row_count, feat_width = local.shape
    partial_sum = jnp.dot(context, w_out, preferred_element_type=jnp.float32)
    attended = scatter_sum_tp(partial_sum.astype(jnp.bfloat16))
    summed = local.astype(jnp.float32) + attended
    first_sum, square_sum = sum_tp(
        jnp.stack([jnp.sum(summed, axis=1), jnp.sum(summed * summed, axis=1)])
    )
    row_mean = first_sum / D
    row_var = square_sum / D - row_mean * row_mean
    offset = lax.axis_index("tp") * feat_width
    gain_part = lax.dynamic_slice_in_dim(ln_gain, offset, feat_width, 0)
    bias_part = lax.dynamic_slice_in_dim(ln_bias, offset, feat_width, 0)
    scaled = (summed - row_mean[:, None]) / jnp.sqrt(row_var[:, None] + 1e-05)
    return (scaled * gain_part + bias_part).astype(jnp.bfloat16)


def shards(
    tokens, placement, cache_len, w_query, w_key, w_value, w_out, k_cache, v_cache, ln_gain, ln_bias
):
    row_count, feat_width = tokens.shape
    block_count = placement.shape[0]
    block_rows = row_count // block_count
    per_peer = block_count // lax.axis_size("req")
    send_slot = placement // block_count * per_peer + placement % per_peer
    send_order = (
        jnp.zeros((block_count,), jnp.int32)
        .at[send_slot]
        .set(jnp.arange(block_count, dtype=jnp.int32))
    )

    def to_blocks(array):
        return array.reshape(block_count, block_rows, array.shape[1])

    arrived = lax.all_to_all(
        to_blocks(tokens)[send_order], "req", split_axis=0, concat_axis=0, tiled=True
    ).reshape(row_count, feat_width)
    whole = gather_tp(arrived)
    queries, new_keys, new_values = project_rows(whole, w_query, w_key, w_value)
    context = attend_all(queries, new_keys, new_values, k_cache, v_cache, cache_len)
    normed = finish_rows(context, arrived, w_out, ln_gain, ln_bias)
    returned = lax.all_to_all(to_blocks(normed), "req", split_axis=0, concat_axis=0, tiled=True)
    return returned[send_slot].reshape(row_count, feat_width)


def solution(mesh):
    in_specs = (
        P("req", "tp"),
        P("req"),
        P("req"),
        P(None, "tp"),
        P(None, "tp"),
        P(None, "tp"),
        P("tp", None),
        P("req", None, "tp"),
        P("req", None, "tp"),
        P(),
        P(),
    )
    out_specs = P("req", "tp")
    return jax.shard_map(shards, mesh=mesh, in_specs=in_specs, out_specs=out_specs, check_vma=False)
```

```python
import jax
import jax.numpy as jnp
from jax import lax
from jax.sharding import PartitionSpec as P

D = 1024
HEADS = 16


def gather_tp(part):
    count = lax.axis_size("tp")
    copies = jnp.broadcast_to(part[None], (count,) + part.shape)
    got = lax.all_to_all(copies, "tp", 0, 0, tiled=True)
    return jnp.moveaxis(got, 0, 1).reshape(part.shape[0], count * part.shape[1])


def scatter_sum_tp(whole):
    count = lax.axis_size("tp")
    rows, width = whole.shape
    pieces = jnp.moveaxis(whole.reshape(rows, count, width // count), 1, 0)
    got = lax.all_to_all(pieces, "tp", 0, 0, tiled=True)
    return jnp.sum(got.astype(jnp.float32), axis=0)


def sum_tp(stats):
    count = lax.axis_size("tp")
    copies = jnp.broadcast_to(stats[None], (count,) + stats.shape)
    got = lax.all_to_all(copies, "tp", 0, 0, tiled=True)
    return jnp.sum(got, axis=0)


def head_view(array, head_size):
    return array.reshape(array.shape[0], array.shape[1] // head_size, head_size)


def attend_padded(queries, new_keys, new_values, cache_keys, cache_values, length):
    head_size = D // HEADS
    new_count = queries.shape[0]
    span = cache_keys.shape[0]
    keys_all = head_view(jnp.concatenate([cache_keys, new_keys], 0), head_size)
    values_all = head_view(jnp.concatenate([cache_values, new_values], 0), head_size)
    query_heads = head_view(queries, head_size)
    scores = jnp.einsum(
        "qhd,khd->hqk", query_heads, keys_all, preferred_element_type=jnp.float32
    ) * head_size ** (-0.5)
    key_pos = jnp.arange(span + new_count, dtype=jnp.int32)[None, :]
    query_pos = jnp.arange(new_count, dtype=jnp.int32)[:, None]
    valid = jnp.where(key_pos < span, key_pos < length, key_pos - span <= query_pos)
    scores = jnp.where(valid[None], scores, -jnp.inf)
    top = jnp.max(scores, axis=-1, keepdims=True)
    weight = jnp.where(valid[None], jnp.exp(scores - top), 0.0)
    total = jnp.sum(weight, axis=-1)
    context = jnp.einsum(
        "hqk,khd->qhd", weight.astype(jnp.bfloat16), values_all, preferred_element_type=jnp.float32
    )
    context = context / jnp.transpose(total)[:, :, None]
    return context.reshape(new_count, queries.shape[1]).astype(jnp.bfloat16)


def attend_all(queries, new_keys, new_values, k_cache, v_cache, cache_len):
    request_count = k_cache.shape[0]
    req_shape = (request_count, queries.shape[0] // request_count, queries.shape[1])
    span = req_shape[1]
    parts = [
        attend_padded(
            queries[g * span:(g + 1) * span],
            new_keys[g * span:(g + 1) * span],
            new_values[g * span:(g + 1) * span],
            k_cache[g],
            v_cache[g],
            cache_len[g],
        )
        for g in range(request_count)
    ]
    return jnp.concatenate(parts, 0)


def project_rows(whole, w_query, w_key, w_value):
    queries = jnp.dot(whole, w_query, preferred_element_type=jnp.float32).astype(jnp.bfloat16)
    new_keys = jnp.dot(whole, w_key, preferred_element_type=jnp.float32).astype(jnp.bfloat16)
    new_values = jnp.dot(whole, w_value, preferred_element_type=jnp.float32).astype(jnp.bfloat16)
    return (queries, new_keys, new_values)


def finish_rows(context, local, w_out, ln_gain, ln_bias):
    row_count, feat_width = local.shape
    partial_sum = jnp.dot(context, w_out, preferred_element_type=jnp.float32)
    attended = scatter_sum_tp(partial_sum.astype(jnp.bfloat16))
    summed = local.astype(jnp.float32) + attended
    first_sum, square_sum = sum_tp(
        jnp.stack([jnp.sum(summed, axis=1), jnp.sum(summed * summed, axis=1)])
    )
    row_mean = first_sum / D
    row_var = square_sum / D - row_mean * row_mean
    offset = lax.axis_index("tp") * feat_width
    gain_part = lax.dynamic_slice_in_dim(ln_gain, offset, feat_width, 0)
    bias_part = lax.dynamic_slice_in_dim(ln_bias, offset, feat_width, 0)
    scaled = (summed - row_mean[:, None]) / jnp.sqrt(row_var[:, None] + 1e-05)
    return (scaled * gain_part + bias_part).astype(jnp.bfloat16)


def shards(
    tokens, placement, cache_len, w_query, w_key, w_value, w_out, k_cache, v_cache, ln_gain, ln_bias
):
    row_count, feat_width = tokens.shape
    block_count = placement.shape[0]
    block_rows = row_count // block_count
    per_peer = block_count // lax.axis_size("req")
    send_slot = placement // block_count * per_peer + placement % per_peer
    send_order = (
        jnp.zeros((block_count,), jnp.int32)
        .at[send_slot]
        .set(jnp.arange(block_count, dtype=jnp.int32))
    )

    def to_blocks(array):
        return array.reshape(block_count, block_rows, array.shape[1])

    arrived = lax.all_to_all(
        to_blocks(tokens)[send_order], "req", split_axis=0, concat_axis=0, tiled=True
    ).reshape(row_count, feat_width)
    whole = gather_tp(arrived)
    queries, new_keys, new_values = project_rows(whole, w_query, w_key, w_value)
    context = attend_all(queries, new_keys, new_values, k_cache, v_cache, cache_len)
    normed = finish_rows(context, arrived, w_out, ln_gain, ln_bias)
    returned = lax.all_to_all(to_blocks(normed), "req", split_axis=0, concat_axis=0, tiled=True)
    return returned[send_slot].reshape(row_count, feat_width)


def solution(mesh):
    in_specs = (
        P("req", "tp"),
        P("req"),
        P("req"),
        P(None, "tp"),
        P(None, "tp"),
        P(None, "tp"),
        P("tp", None),
        P("req", None, "tp"),
        P("req", None, "tp"),
        P(),
        P(),
    )
    out_specs = P("req", "tp")
    return jax.shard_map(shards, mesh=mesh, in_specs=in_specs, out_specs=out_specs, check_vma=False)
```

```python
import jax
import jax.numpy as jnp
from jax import lax
from jax.sharding import PartitionSpec as P

D = 1024
HEADS = 16


def gather_tp(part):
    count = lax.axis_size("tp")
    copies = jnp.broadcast_to(part[None], (count,) + part.shape)
    got = lax.all_to_all(copies, "tp", 0, 0, tiled=True)
    return jnp.moveaxis(got, 0, 1).reshape(part.shape[0], count * part.shape[1])


def scatter_sum_tp(whole):
    count = lax.axis_size("tp")
    rows, width = whole.shape
    pieces = jnp.moveaxis(whole.reshape(rows, count, width // count), 1, 0)
    got = lax.all_to_all(pieces, "tp", 0, 0, tiled=True)
    return jnp.sum(got.astype(jnp.float32), axis=0)


def sum_tp(stats):
    count = lax.axis_size("tp")
    copies = jnp.broadcast_to(stats[None], (count,) + stats.shape)
    got = lax.all_to_all(copies, "tp", 0, 0, tiled=True)
    return jnp.sum(got, axis=0)


def head_view(array, head_size):
    return array.reshape(array.shape[0], array.shape[1] // head_size, head_size)


def attend_padded(queries, new_keys, new_values, cache_keys, cache_values, length):
    head_size = D // HEADS
    new_count = queries.shape[0]
    span = cache_keys.shape[0]
    keys_all = head_view(jnp.concatenate([cache_keys, new_keys], 0), head_size)
    values_all = head_view(jnp.concatenate([cache_values, new_values], 0), head_size)
    query_heads = head_view(queries, head_size)
    scores = jnp.einsum(
        "qhd,khd->hqk", query_heads, keys_all, preferred_element_type=jnp.float32
    ) * head_size ** (-0.5)
    key_pos = jnp.arange(span + new_count, dtype=jnp.int32)[None, :]
    query_pos = jnp.arange(new_count, dtype=jnp.int32)[:, None]
    valid = jnp.where(key_pos < span, key_pos < length, key_pos - span <= query_pos)
    scores = jnp.where(valid[None], scores, -jnp.inf)
    top = jnp.max(scores, axis=-1, keepdims=True)
    weight = jnp.where(valid[None], jnp.exp(scores - top), 0.0)
    total = jnp.sum(weight, axis=-1)
    context = jnp.einsum(
        "hqk,khd->qhd", weight.astype(jnp.bfloat16), values_all, preferred_element_type=jnp.float32
    )
    context = context / jnp.transpose(total)[:, :, None]
    return context.reshape(new_count, queries.shape[1]).astype(jnp.bfloat16)


def attend_all(queries, new_keys, new_values, k_cache, v_cache, cache_len):
    request_count = k_cache.shape[0]
    req_shape = (request_count, queries.shape[0] // request_count, queries.shape[1])
    span = req_shape[1]
    parts = [
        attend_padded(
            queries[g * span:(g + 1) * span],
            new_keys[g * span:(g + 1) * span],
            new_values[g * span:(g + 1) * span],
            k_cache[g],
            v_cache[g],
            cache_len[g],
        )
        for g in range(request_count)
    ]
    return jnp.concatenate(parts, 0)


def project_rows(whole, w_query, w_key, w_value):
    queries = jnp.dot(whole, w_query, preferred_element_type=jnp.float32).astype(jnp.bfloat16)
    new_keys = jnp.dot(whole, w_key, preferred_element_type=jnp.float32).astype(jnp.bfloat16)
    new_values = jnp.dot(whole, w_value, preferred_element_type=jnp.float32).astype(jnp.bfloat16)
    return (queries, new_keys, new_values)


def finish_rows(context, local, w_out, ln_gain, ln_bias):
    row_count, feat_width = local.shape
    partial_sum = jnp.dot(context, w_out, preferred_element_type=jnp.float32)
    attended = scatter_sum_tp(partial_sum.astype(jnp.bfloat16))
    summed = local.astype(jnp.float32) + attended
    first_sum, square_sum = sum_tp(
        jnp.stack([jnp.sum(summed, axis=1), jnp.sum(summed * summed, axis=1)])
    )
    row_mean = first_sum / D
    row_var = square_sum / D - row_mean * row_mean
    offset = lax.axis_index("tp") * feat_width
    gain_part = lax.dynamic_slice_in_dim(ln_gain, offset, feat_width, 0)
    bias_part = lax.dynamic_slice_in_dim(ln_bias, offset, feat_width, 0)
    scaled = (summed - row_mean[:, None]) / jnp.sqrt(row_var[:, None] + 1e-05)
    return (scaled * gain_part + bias_part).astype(jnp.bfloat16)


def shards(
    tokens, placement, cache_len, w_query, w_key, w_value, w_out, k_cache, v_cache, ln_gain, ln_bias
):
    row_count, feat_width = tokens.shape
    block_count = placement.shape[0]
    block_rows = row_count // block_count
    per_peer = block_count // lax.axis_size("req")
    send_slot = placement // block_count * per_peer + placement % per_peer
    choose = (
        send_slot[None, :] == jnp.arange(block_count, dtype=jnp.int32)[:, None]
    ).astype(jnp.bfloat16)

    def to_blocks(array):
        return array.reshape(block_count, block_rows, array.shape[1])

    ordered = jnp.einsum(
        "ja,aif->jif", choose, to_blocks(tokens), preferred_element_type=jnp.float32
    ).astype(jnp.bfloat16)
    arrived = lax.all_to_all(
        ordered, "req", split_axis=0, concat_axis=0, tiled=True
    ).reshape(row_count, feat_width)
    whole = gather_tp(arrived)
    queries, new_keys, new_values = project_rows(whole, w_query, w_key, w_value)
    context = attend_all(queries, new_keys, new_values, k_cache, v_cache, cache_len)
    normed = finish_rows(context, arrived, w_out, ln_gain, ln_bias)
    returned = lax.all_to_all(to_blocks(normed), "req", split_axis=0, concat_axis=0, tiled=True)
    back = jnp.einsum("ja,jif->aif", choose, returned, preferred_element_type=jnp.float32)
    return back.astype(jnp.bfloat16).reshape(row_count, feat_width)


def solution(mesh):
    in_specs = (
        P("req", "tp"),
        P("req"),
        P("req"),
        P(None, "tp"),
        P(None, "tp"),
        P(None, "tp"),
        P("tp", None),
        P("req", None, "tp"),
        P("req", None, "tp"),
        P(),
        P(),
    )
    out_specs = P("req", "tp")
    return jax.shard_map(shards, mesh=mesh, in_specs=in_specs, out_specs=out_specs, check_vma=False)
```

```python
import jax
import jax.numpy as jnp
from jax import lax
from jax.experimental import pallas as pl
from jax.experimental.pallas import tpu as pltpu
from jax.sharding import PartitionSpec as P

D = 1024
HEADS = 16


def gather_tp(part):
    count = lax.axis_size("tp")
    copies = jnp.broadcast_to(part[None], (count,) + part.shape)
    got = lax.all_to_all(copies, "tp", 0, 0, tiled=True)
    return jnp.moveaxis(got, 0, 1).reshape(part.shape[0], count * part.shape[1])


def scatter_sum_tp(whole):
    count = lax.axis_size("tp")
    rows, width = whole.shape
    pieces = jnp.moveaxis(whole.reshape(rows, count, width // count), 1, 0)
    got = lax.all_to_all(pieces, "tp", 0, 0, tiled=True)
    return jnp.sum(got.astype(jnp.float32), axis=0)


def sum_tp(stats):
    count = lax.axis_size("tp")
    copies = jnp.broadcast_to(stats[None], (count,) + stats.shape)
    got = lax.all_to_all(copies, "tp", 0, 0, tiled=True)
    return jnp.sum(got, axis=0)


HEAD = 64


def attend_kernel(lens_ref, q_ref, kn_ref, vn_ref, kc_ref, vc_ref, out_ref):
    g = pl.program_id(0)
    length = lens_ref[g]
    new_count = q_ref.shape[1]
    span = kc_ref.shape[1]
    heads = q_ref.shape[2] // HEAD
    cache_pos = lax.broadcasted_iota(jnp.int32, (new_count, span), 1)
    cache_ok = cache_pos < length
    row = lax.broadcasted_iota(jnp.int32, (new_count, new_count), 0)
    col = lax.broadcasted_iota(jnp.int32, (new_count, new_count), 1)
    new_ok = col <= row
    dims = (((1,), (1,)), ((), ()))
    for h in range(heads):
        cols = slice(h * HEAD, (h + 1) * HEAD)
        qh = q_ref[0, :, cols]
        sc = lax.dot_general(qh, kc_ref[0, :, cols], dims, preferred_element_type=jnp.float32) * HEAD ** (-0.5)
        sn = lax.dot_general(qh, kn_ref[0, :, cols], dims, preferred_element_type=jnp.float32) * HEAD ** (-0.5)
        sc = jnp.where(cache_ok, sc, -jnp.inf)
        sn = jnp.where(new_ok, sn, -jnp.inf)
        top = jnp.maximum(jnp.max(sc, axis=1, keepdims=True), jnp.max(sn, axis=1, keepdims=True))
        wc = jnp.where(cache_ok, jnp.exp(sc - top), 0.0)
        wn = jnp.where(new_ok, jnp.exp(sn - top), 0.0)
        total = jnp.sum(wc, axis=1, keepdims=True) + jnp.sum(wn, axis=1, keepdims=True)
        ctx = jnp.dot(wc.astype(jnp.bfloat16), vc_ref[0, :, cols], preferred_element_type=jnp.float32)
        ctx = ctx + jnp.dot(wn.astype(jnp.bfloat16), vn_ref[0, :, cols], preferred_element_type=jnp.float32)
        out_ref[0, :, cols] = (ctx / total).astype(out_ref.dtype)


def attend_pallas(queries, new_keys, new_values, k_cache, v_cache, cache_len):
    requests, span, width = k_cache.shape
    new_count = queries.shape[0] // requests
    shape3 = (requests, new_count, width)
    q3, kn3, vn3 = (a.reshape(shape3) for a in (queries, new_keys, new_values))
    new_spec = pl.BlockSpec((1, new_count, width), lambda g, lens: (g, 0, 0))
    cache_spec = pl.BlockSpec((1, span, width), lambda g, lens: (g, 0, 0))
    out = pl.pallas_call(
        attend_kernel,
        out_shape=jax.ShapeDtypeStruct(shape3, jnp.bfloat16),
        grid_spec=pltpu.PrefetchScalarGridSpec(
            num_scalar_prefetch=1,
            grid=(requests,),
            in_specs=[new_spec, new_spec, new_spec, cache_spec, cache_spec],
            out_specs=new_spec,
        ),
    )(cache_len, q3, kn3, vn3, k_cache, v_cache)
    return out.reshape(queries.shape)


def head_view(array, head_size):
    return array.reshape(array.shape[0], array.shape[1] // head_size, head_size)


def attend_padded(queries, new_keys, new_values, cache_keys, cache_values, length):
    head_size = D // HEADS
    new_count = queries.shape[0]
    span = cache_keys.shape[0]
    keys_all = head_view(jnp.concatenate([cache_keys, new_keys], 0), head_size)
    values_all = head_view(jnp.concatenate([cache_values, new_values], 0), head_size)
    query_heads = head_view(queries, head_size)
    scores = jnp.einsum(
        "qhd,khd->hqk", query_heads, keys_all, preferred_element_type=jnp.float32
    ) * head_size ** (-0.5)
    key_pos = jnp.arange(span + new_count, dtype=jnp.int32)[None, :]
    query_pos = jnp.arange(new_count, dtype=jnp.int32)[:, None]
    valid = jnp.where(key_pos < span, key_pos < length, key_pos - span <= query_pos)
    scores = jnp.where(valid[None], scores, -jnp.inf)
    top = jnp.max(scores, axis=-1, keepdims=True)
    weight = jnp.where(valid[None], jnp.exp(scores - top), 0.0)
    total = jnp.sum(weight, axis=-1)
    context = jnp.einsum(
        "hqk,khd->qhd", weight.astype(jnp.bfloat16), values_all, preferred_element_type=jnp.float32
    )
    context = context / jnp.transpose(total)[:, :, None]
    return context.reshape(new_count, queries.shape[1]).astype(jnp.bfloat16)


def attend_all(queries, new_keys, new_values, k_cache, v_cache, cache_len):
    request_count = k_cache.shape[0]
    req_shape = (request_count, queries.shape[0] // request_count, queries.shape[1])
    span = req_shape[1]
    parts = [
        attend_padded(
            queries[g * span:(g + 1) * span],
            new_keys[g * span:(g + 1) * span],
            new_values[g * span:(g + 1) * span],
            k_cache[g],
            v_cache[g],
            cache_len[g],
        )
        for g in range(request_count)
    ]
    return jnp.concatenate(parts, 0)


def project_rows(whole, w_query, w_key, w_value):
    queries = jnp.dot(whole, w_query, preferred_element_type=jnp.float32).astype(jnp.bfloat16)
    new_keys = jnp.dot(whole, w_key, preferred_element_type=jnp.float32).astype(jnp.bfloat16)
    new_values = jnp.dot(whole, w_value, preferred_element_type=jnp.float32).astype(jnp.bfloat16)
    return (queries, new_keys, new_values)


def finish_rows(context, local, w_out, ln_gain, ln_bias):
    row_count, feat_width = local.shape
    partial_sum = jnp.dot(context, w_out, preferred_element_type=jnp.float32)
    attended = scatter_sum_tp(partial_sum.astype(jnp.bfloat16))
    summed = local.astype(jnp.float32) + attended
    first_sum, square_sum = sum_tp(
        jnp.stack([jnp.sum(summed, axis=1), jnp.sum(summed * summed, axis=1)])
    )
    row_mean = first_sum / D
    row_var = square_sum / D - row_mean * row_mean
    offset = lax.axis_index("tp") * feat_width
    gain_part = lax.dynamic_slice_in_dim(ln_gain, offset, feat_width, 0)
    bias_part = lax.dynamic_slice_in_dim(ln_bias, offset, feat_width, 0)
    scaled = (summed - row_mean[:, None]) / jnp.sqrt(row_var[:, None] + 1e-05)
    return (scaled * gain_part + bias_part).astype(jnp.bfloat16)


def shards(
    tokens, placement, cache_len, w_query, w_key, w_value, w_out, k_cache, v_cache, ln_gain, ln_bias
):
    row_count, feat_width = tokens.shape
    block_count = placement.shape[0]
    block_rows = row_count // block_count
    per_peer = block_count // lax.axis_size("req")
    send_slot = placement // block_count * per_peer + placement % per_peer
    choose = (
        send_slot[None, :] == jnp.arange(block_count, dtype=jnp.int32)[:, None]
    ).astype(jnp.bfloat16)

    def to_blocks(array):
        return array.reshape(block_count, block_rows, array.shape[1])

    ordered = jnp.einsum(
        "ja,aif->jif", choose, to_blocks(tokens), preferred_element_type=jnp.float32
    ).astype(jnp.bfloat16)
    arrived = lax.all_to_all(
        ordered, "req", split_axis=0, concat_axis=0, tiled=True
    ).reshape(row_count, feat_width)
    whole = gather_tp(arrived)
    queries, new_keys, new_values = project_rows(whole, w_query, w_key, w_value)
    context = attend_pallas(queries, new_keys, new_values, k_cache, v_cache, cache_len)
    normed = finish_rows(context, arrived, w_out, ln_gain, ln_bias)
    returned = lax.all_to_all(to_blocks(normed), "req", split_axis=0, concat_axis=0, tiled=True)
    back = jnp.einsum("ja,jif->aif", choose, returned, preferred_element_type=jnp.float32)
    return back.astype(jnp.bfloat16).reshape(row_count, feat_width)


def solution(mesh):
    in_specs = (
        P("req", "tp"),
        P("req"),
        P("req"),
        P(None, "tp"),
        P(None, "tp"),
        P(None, "tp"),
        P("tp", None),
        P("req", None, "tp"),
        P("req", None, "tp"),
        P(),
        P(),
    )
    out_specs = P("req", "tp")
    return jax.shard_map(shards, mesh=mesh, in_specs=in_specs, out_specs=out_specs, check_vma=False)
```

```python
import jax
import jax.numpy as jnp
from jax import lax
from jax.experimental import pallas as pl
from jax.experimental.pallas import tpu as pltpu
from jax.sharding import PartitionSpec as P

D = 1024
HEADS = 16


def gather_tp(part):
    count = lax.axis_size("tp")
    copies = jnp.broadcast_to(part[None], (count,) + part.shape)
    got = lax.all_to_all(copies, "tp", 0, 0, tiled=True)
    return jnp.moveaxis(got, 0, 1).reshape(part.shape[0], count * part.shape[1])


def scatter_sum_tp(whole):
    count = lax.axis_size("tp")
    rows, width = whole.shape
    pieces = jnp.moveaxis(whole.reshape(rows, count, width // count), 1, 0)
    got = lax.all_to_all(pieces, "tp", 0, 0, tiled=True)
    return jnp.sum(got.astype(jnp.float32), axis=0)


def sum_tp(stats):
    count = lax.axis_size("tp")
    copies = jnp.broadcast_to(stats[None], (count,) + stats.shape)
    got = lax.all_to_all(copies, "tp", 0, 0, tiled=True)
    return jnp.sum(got, axis=0)


HEAD = 64


def attend_kernel(lens_ref, q_ref, kn_ref, vn_ref, kc_ref, vc_ref, out_ref):
    g = pl.program_id(0)
    length = lens_ref[g]
    new_count = q_ref.shape[1]
    span = kc_ref.shape[1]
    heads = q_ref.shape[2] // HEAD
    cache_pos = lax.broadcasted_iota(jnp.int32, (new_count, span), 1)
    cache_ok = cache_pos < length
    row = lax.broadcasted_iota(jnp.int32, (new_count, new_count), 0)
    col = lax.broadcasted_iota(jnp.int32, (new_count, new_count), 1)
    new_ok = col <= row
    dims = (((1,), (1,)), ((), ()))
    for h in range(heads):
        cols = slice(h * HEAD, (h + 1) * HEAD)
        qh = q_ref[0, :, cols]
        sc = lax.dot_general(qh, kc_ref[0, :, cols], dims, preferred_element_type=jnp.float32) * HEAD ** (-0.5)
        sn = lax.dot_general(qh, kn_ref[0, :, cols], dims, preferred_element_type=jnp.float32) * HEAD ** (-0.5)
        sc = jnp.where(cache_ok, sc, -jnp.inf)
        sn = jnp.where(new_ok, sn, -jnp.inf)
        top = jnp.maximum(jnp.max(sc, axis=1, keepdims=True), jnp.max(sn, axis=1, keepdims=True))
        wc = jnp.exp(sc - top)
        wn = jnp.exp(sn - top)
        total = jnp.sum(wc, axis=1, keepdims=True) + jnp.sum(wn, axis=1, keepdims=True)
        ctx = jnp.dot(wc.astype(jnp.bfloat16), vc_ref[0, :, cols], preferred_element_type=jnp.float32)
        ctx = ctx + jnp.dot(wn.astype(jnp.bfloat16), vn_ref[0, :, cols], preferred_element_type=jnp.float32)
        out_ref[0, :, cols] = (ctx / total).astype(out_ref.dtype)


def attend_pallas(queries, new_keys, new_values, k_cache, v_cache, cache_len):
    requests, span, width = k_cache.shape
    new_count = queries.shape[0] // requests
    shape3 = (requests, new_count, width)
    q3, kn3, vn3 = (a.reshape(shape3) for a in (queries, new_keys, new_values))
    new_spec = pl.BlockSpec((1, new_count, width), lambda g, lens: (g, 0, 0))
    cache_spec = pl.BlockSpec((1, span, width), lambda g, lens: (g, 0, 0))
    out = pl.pallas_call(
        attend_kernel,
        out_shape=jax.ShapeDtypeStruct(shape3, jnp.bfloat16),
        grid_spec=pltpu.PrefetchScalarGridSpec(
            num_scalar_prefetch=1,
            grid=(requests,),
            in_specs=[new_spec, new_spec, new_spec, cache_spec, cache_spec],
            out_specs=new_spec,
        ),
    )(cache_len, q3, kn3, vn3, k_cache, v_cache)
    return out.reshape(queries.shape)


def head_view(array, head_size):
    return array.reshape(array.shape[0], array.shape[1] // head_size, head_size)


def attend_padded(queries, new_keys, new_values, cache_keys, cache_values, length):
    head_size = D // HEADS
    new_count = queries.shape[0]
    span = cache_keys.shape[0]
    keys_all = head_view(jnp.concatenate([cache_keys, new_keys], 0), head_size)
    values_all = head_view(jnp.concatenate([cache_values, new_values], 0), head_size)
    query_heads = head_view(queries, head_size)
    scores = jnp.einsum(
        "qhd,khd->hqk", query_heads, keys_all, preferred_element_type=jnp.float32
    ) * head_size ** (-0.5)
    key_pos = jnp.arange(span + new_count, dtype=jnp.int32)[None, :]
    query_pos = jnp.arange(new_count, dtype=jnp.int32)[:, None]
    valid = jnp.where(key_pos < span, key_pos < length, key_pos - span <= query_pos)
    scores = jnp.where(valid[None], scores, -jnp.inf)
    top = jnp.max(scores, axis=-1, keepdims=True)
    weight = jnp.where(valid[None], jnp.exp(scores - top), 0.0)
    total = jnp.sum(weight, axis=-1)
    context = jnp.einsum(
        "hqk,khd->qhd", weight.astype(jnp.bfloat16), values_all, preferred_element_type=jnp.float32
    )
    context = context / jnp.transpose(total)[:, :, None]
    return context.reshape(new_count, queries.shape[1]).astype(jnp.bfloat16)


def attend_all(queries, new_keys, new_values, k_cache, v_cache, cache_len):
    request_count = k_cache.shape[0]
    req_shape = (request_count, queries.shape[0] // request_count, queries.shape[1])
    span = req_shape[1]
    parts = [
        attend_padded(
            queries[g * span:(g + 1) * span],
            new_keys[g * span:(g + 1) * span],
            new_values[g * span:(g + 1) * span],
            k_cache[g],
            v_cache[g],
            cache_len[g],
        )
        for g in range(request_count)
    ]
    return jnp.concatenate(parts, 0)


def project_rows(whole, w_query, w_key, w_value):
    width = w_query.shape[1]
    joined = jnp.concatenate([w_query, w_key, w_value], 1)
    all_three = jnp.dot(whole, joined, preferred_element_type=jnp.float32).astype(jnp.bfloat16)
    return (all_three[:, :width], all_three[:, width:2 * width], all_three[:, 2 * width:])


def finish_rows(context, local, w_out, ln_gain, ln_bias):
    row_count, feat_width = local.shape
    partial_sum = jnp.dot(context, w_out, preferred_element_type=jnp.float32)
    attended = scatter_sum_tp(partial_sum.astype(jnp.bfloat16))
    summed = local.astype(jnp.float32) + attended
    first_sum, square_sum = sum_tp(
        jnp.stack([jnp.sum(summed, axis=1), jnp.sum(summed * summed, axis=1)])
    )
    row_mean = first_sum / D
    row_var = square_sum / D - row_mean * row_mean
    offset = lax.axis_index("tp") * feat_width
    gain_part = lax.dynamic_slice_in_dim(ln_gain, offset, feat_width, 0)
    bias_part = lax.dynamic_slice_in_dim(ln_bias, offset, feat_width, 0)
    scaled = (summed - row_mean[:, None]) / jnp.sqrt(row_var[:, None] + 1e-05)
    return (scaled * gain_part + bias_part).astype(jnp.bfloat16)


def shards(
    tokens, placement, cache_len, w_query, w_key, w_value, w_out, k_cache, v_cache, ln_gain, ln_bias
):
    row_count, feat_width = tokens.shape
    block_count = placement.shape[0]
    block_rows = row_count // block_count
    per_peer = block_count // lax.axis_size("req")
    send_slot = placement // block_count * per_peer + placement % per_peer
    choose = (
        send_slot[None, :] == jnp.arange(block_count, dtype=jnp.int32)[:, None]
    ).astype(jnp.bfloat16)

    def to_blocks(array):
        return array.reshape(block_count, block_rows, array.shape[1])

    ordered = jnp.einsum(
        "ja,aif->jif", choose, to_blocks(tokens), preferred_element_type=jnp.float32
    ).astype(jnp.bfloat16)
    arrived = lax.all_to_all(
        ordered, "req", split_axis=0, concat_axis=0, tiled=True
    ).reshape(row_count, feat_width)
    whole = gather_tp(arrived)
    queries, new_keys, new_values = project_rows(whole, w_query, w_key, w_value)
    context = attend_pallas(queries, new_keys, new_values, k_cache, v_cache, cache_len)
    normed = finish_rows(context, arrived, w_out, ln_gain, ln_bias)
    returned = lax.all_to_all(to_blocks(normed), "req", split_axis=0, concat_axis=0, tiled=True)
    back = jnp.einsum("ja,jif->aif", choose, returned, preferred_element_type=jnp.float32)
    return back.astype(jnp.bfloat16).reshape(row_count, feat_width)


def solution(mesh):
    in_specs = (
        P("req", "tp"),
        P("req"),
        P("req"),
        P(None, "tp"),
        P(None, "tp"),
        P(None, "tp"),
        P("tp", None),
        P("req", None, "tp"),
        P("req", None, "tp"),
        P(),
        P(),
    )
    out_specs = P("req", "tp")
    return jax.shard_map(shards, mesh=mesh, in_specs=in_specs, out_specs=out_specs, check_vma=False)
```

```python
import jax
import jax.numpy as jnp
from jax import lax
from jax.experimental import pallas as pl
from jax.experimental.pallas import tpu as pltpu
from jax.sharding import PartitionSpec as P

D = 1024
HEADS = 16


def gather_tp(part):
    count = lax.axis_size("tp")
    copies = jnp.broadcast_to(part[None], (count,) + part.shape)
    got = lax.all_to_all(copies, "tp", 0, 0, tiled=True)
    return jnp.moveaxis(got, 0, 1).reshape(part.shape[0], count * part.shape[1])


def scatter_sum_tp(whole):
    count = lax.axis_size("tp")
    rows, width = whole.shape
    pieces = jnp.moveaxis(whole.reshape(rows, count, width // count), 1, 0)
    got = lax.all_to_all(pieces, "tp", 0, 0, tiled=True)
    return jnp.sum(got.astype(jnp.float32), axis=0)


def sum_tp(stats):
    count = lax.axis_size("tp")
    copies = jnp.broadcast_to(stats[None], (count,) + stats.shape)
    got = lax.all_to_all(copies, "tp", 0, 0, tiled=True)
    return jnp.sum(got, axis=0)


HEAD = 64


def attend_kernel(lens_ref, rows_ref, wj_ref, kc_ref, vc_ref, wo_ref, out_ref):
    g = pl.program_id(0)
    length = lens_ref[g]
    new_count = rows_ref.shape[1]
    span = kc_ref.shape[1]
    width = kc_ref.shape[2]
    heads = width // HEAD
    qkv = jnp.dot(rows_ref[0], wj_ref[...], preferred_element_type=jnp.float32).astype(jnp.bfloat16)
    cache_pos = lax.broadcasted_iota(jnp.int32, (new_count, span), 1)
    cache_ok = cache_pos < length
    row = lax.broadcasted_iota(jnp.int32, (new_count, new_count), 0)
    col = lax.broadcasted_iota(jnp.int32, (new_count, new_count), 1)
    new_ok = col <= row
    dims = (((1,), (1,)), ((), ()))
    parts = []
    for h in range(heads):
        cols = slice(h * HEAD, (h + 1) * HEAD)
        qh = qkv[:, h * HEAD:(h + 1) * HEAD]
        kn = qkv[:, width + h * HEAD:width + (h + 1) * HEAD]
        vn = qkv[:, 2 * width + h * HEAD:2 * width + (h + 1) * HEAD]
        sc = lax.dot_general(qh, kc_ref[0, :, cols], dims, preferred_element_type=jnp.float32) * HEAD ** (-0.5)
        sn = lax.dot_general(qh, kn, dims, preferred_element_type=jnp.float32) * HEAD ** (-0.5)
        sc = jnp.where(cache_ok, sc, -jnp.inf)
        sn = jnp.where(new_ok, sn, -jnp.inf)
        top = jnp.maximum(jnp.max(sc, axis=1, keepdims=True), jnp.max(sn, axis=1, keepdims=True))
        wc = jnp.exp(sc - top)
        wn = jnp.exp(sn - top)
        total = jnp.sum(wc, axis=1, keepdims=True) + jnp.sum(wn, axis=1, keepdims=True)
        ctx = jnp.dot(wc.astype(jnp.bfloat16), vc_ref[0, :, cols], preferred_element_type=jnp.float32)
        ctx = ctx + jnp.dot(wn.astype(jnp.bfloat16), vn, preferred_element_type=jnp.float32)
        parts.append((ctx / total).astype(jnp.bfloat16))
    context = jnp.concatenate(parts, axis=1)
    out_ref[0] = jnp.dot(context, wo_ref[...], preferred_element_type=jnp.float32).astype(out_ref.dtype)


def attend_pallas(whole, w_joined, k_cache, v_cache, w_out, cache_len):
    requests, span, width = k_cache.shape
    new_count = whole.shape[0] // requests
    feats = whole.shape[1]
    rows = whole.reshape(requests, new_count, feats)
    row_spec = pl.BlockSpec((1, new_count, feats), lambda g, lens: (g, 0, 0))
    cache_spec = pl.BlockSpec((1, span, width), lambda g, lens: (g, 0, 0))
    wj_spec = pl.BlockSpec(w_joined.shape, lambda g, lens: (0, 0))
    wo_spec = pl.BlockSpec(w_out.shape, lambda g, lens: (0, 0))
    out_spec = pl.BlockSpec((1, new_count, w_out.shape[1]), lambda g, lens: (g, 0, 0))
    out = pl.pallas_call(
        attend_kernel,
        out_shape=jax.ShapeDtypeStruct((requests, new_count, w_out.shape[1]), jnp.bfloat16),
        grid_spec=pltpu.PrefetchScalarGridSpec(
            num_scalar_prefetch=1,
            grid=(requests,),
            in_specs=[row_spec, wj_spec, cache_spec, cache_spec, wo_spec],
            out_specs=out_spec,
        ),
    )(cache_len, rows, w_joined, k_cache, v_cache, w_out)
    return out.reshape(whole.shape[0], w_out.shape[1])


def head_view(array, head_size):
    return array.reshape(array.shape[0], array.shape[1] // head_size, head_size)


def attend_padded(queries, new_keys, new_values, cache_keys, cache_values, length):
    head_size = D // HEADS
    new_count = queries.shape[0]
    span = cache_keys.shape[0]
    keys_all = head_view(jnp.concatenate([cache_keys, new_keys], 0), head_size)
    values_all = head_view(jnp.concatenate([cache_values, new_values], 0), head_size)
    query_heads = head_view(queries, head_size)
    scores = jnp.einsum(
        "qhd,khd->hqk", query_heads, keys_all, preferred_element_type=jnp.float32
    ) * head_size ** (-0.5)
    key_pos = jnp.arange(span + new_count, dtype=jnp.int32)[None, :]
    query_pos = jnp.arange(new_count, dtype=jnp.int32)[:, None]
    valid = jnp.where(key_pos < span, key_pos < length, key_pos - span <= query_pos)
    scores = jnp.where(valid[None], scores, -jnp.inf)
    top = jnp.max(scores, axis=-1, keepdims=True)
    weight = jnp.where(valid[None], jnp.exp(scores - top), 0.0)
    total = jnp.sum(weight, axis=-1)
    context = jnp.einsum(
        "hqk,khd->qhd", weight.astype(jnp.bfloat16), values_all, preferred_element_type=jnp.float32
    )
    context = context / jnp.transpose(total)[:, :, None]
    return context.reshape(new_count, queries.shape[1]).astype(jnp.bfloat16)


def attend_all(queries, new_keys, new_values, k_cache, v_cache, cache_len):
    request_count = k_cache.shape[0]
    req_shape = (request_count, queries.shape[0] // request_count, queries.shape[1])
    span = req_shape[1]
    parts = [
        attend_padded(
            queries[g * span:(g + 1) * span],
            new_keys[g * span:(g + 1) * span],
            new_values[g * span:(g + 1) * span],
            k_cache[g],
            v_cache[g],
            cache_len[g],
        )
        for g in range(request_count)
    ]
    return jnp.concatenate(parts, 0)


def project_rows(whole, w_query, w_key, w_value):
    width = w_query.shape[1]
    joined = jnp.concatenate([w_query, w_key, w_value], 1)
    all_three = jnp.dot(whole, joined, preferred_element_type=jnp.float32).astype(jnp.bfloat16)
    return (all_three[:, :width], all_three[:, width:2 * width], all_three[:, 2 * width:])


def finish_rows(partial_sum, local, ln_gain, ln_bias):
    row_count, feat_width = local.shape
    attended = scatter_sum_tp(partial_sum)
    summed = local.astype(jnp.float32) + attended
    first_sum, square_sum = sum_tp(
        jnp.stack([jnp.sum(summed, axis=1), jnp.sum(summed * summed, axis=1)])
    )
    row_mean = first_sum / D
    row_var = square_sum / D - row_mean * row_mean
    offset = lax.axis_index("tp") * feat_width
    gain_part = lax.dynamic_slice_in_dim(ln_gain, offset, feat_width, 0)
    bias_part = lax.dynamic_slice_in_dim(ln_bias, offset, feat_width, 0)
    scaled = (summed - row_mean[:, None]) / jnp.sqrt(row_var[:, None] + 1e-05)
    return (scaled * gain_part + bias_part).astype(jnp.bfloat16)


def shards(
    tokens, placement, cache_len, w_query, w_key, w_value, w_out, k_cache, v_cache, ln_gain, ln_bias
):
    row_count, feat_width = tokens.shape
    block_count = placement.shape[0]
    block_rows = row_count // block_count
    per_peer = block_count // lax.axis_size("req")
    send_slot = placement // block_count * per_peer + placement % per_peer
    choose = (
        send_slot[None, :] == jnp.arange(block_count, dtype=jnp.int32)[:, None]
    ).astype(jnp.bfloat16)

    def to_blocks(array):
        return array.reshape(block_count, block_rows, array.shape[1])

    ordered = jnp.einsum(
        "ja,aif->jif", choose, to_blocks(tokens), preferred_element_type=jnp.float32
    ).astype(jnp.bfloat16)
    arrived = lax.all_to_all(
        ordered, "req", split_axis=0, concat_axis=0, tiled=True
    ).reshape(row_count, feat_width)
    whole = gather_tp(arrived)
    w_joined = jnp.concatenate([w_query, w_key, w_value], 1)
    partial_sum = attend_pallas(whole, w_joined, k_cache, v_cache, w_out, cache_len)
    normed = finish_rows(partial_sum, arrived, ln_gain, ln_bias)
    returned = lax.all_to_all(to_blocks(normed), "req", split_axis=0, concat_axis=0, tiled=True)
    back = jnp.einsum("ja,jif->aif", choose, returned, preferred_element_type=jnp.float32)
    return back.astype(jnp.bfloat16).reshape(row_count, feat_width)


def solution(mesh):
    in_specs = (
        P("req", "tp"),
        P("req"),
        P("req"),
        P(None, "tp"),
        P(None, "tp"),
        P(None, "tp"),
        P("tp", None),
        P("req", None, "tp"),
        P("req", None, "tp"),
        P(),
        P(),
    )
    out_specs = P("req", "tp")
    return jax.shard_map(shards, mesh=mesh, in_specs=in_specs, out_specs=out_specs, check_vma=False)
```

```python
import jax
import jax.numpy as jnp
from jax import lax
from jax.experimental import pallas as pl
from jax.experimental.pallas import tpu as pltpu
from jax.sharding import PartitionSpec as P

D = 1024
HEADS = 16


def gather_tp(part):
    count = lax.axis_size("tp")
    copies = jnp.broadcast_to(part[None], (count,) + part.shape)
    got = lax.all_to_all(copies, "tp", 0, 0, tiled=True)
    return jnp.moveaxis(got, 0, 1).reshape(part.shape[0], count * part.shape[1])


def scatter_sum_tp(whole):
    count = lax.axis_size("tp")
    rows, width = whole.shape
    pieces = jnp.moveaxis(whole.reshape(rows, count, width // count), 1, 0)
    got = lax.all_to_all(pieces, "tp", 0, 0, tiled=True)
    return jnp.sum(got.astype(jnp.float32), axis=0)


def sum_tp(stats):
    count = lax.axis_size("tp")
    copies = jnp.broadcast_to(stats[None], (count,) + stats.shape)
    got = lax.all_to_all(copies, "tp", 0, 0, tiled=True)
    return jnp.sum(got, axis=0)


HEAD = 64


def attend_kernel(lens_ref, q_ref, kn_ref, vn_ref, kc_ref, vc_ref, wo_ref, out_ref):
    g = pl.program_id(0)
    length = lens_ref[g]
    new_count = q_ref.shape[1]
    span = kc_ref.shape[1]
    heads = q_ref.shape[2] // HEAD
    cache_pos = lax.broadcasted_iota(jnp.int32, (new_count, span), 1)
    cache_ok = cache_pos < length
    row = lax.broadcasted_iota(jnp.int32, (new_count, new_count), 0)
    col = lax.broadcasted_iota(jnp.int32, (new_count, new_count), 1)
    new_ok = col <= row
    dims = (((1,), (1,)), ((), ()))
    parts = []
    for h in range(heads):
        cols = slice(h * HEAD, (h + 1) * HEAD)
        qh = q_ref[0, :, cols]
        sc = lax.dot_general(qh, kc_ref[0, :, cols], dims, preferred_element_type=jnp.float32) * HEAD ** (-0.5)
        sn = lax.dot_general(qh, kn_ref[0, :, cols], dims, preferred_element_type=jnp.float32) * HEAD ** (-0.5)
        sc = jnp.where(cache_ok, sc, -jnp.inf)
        sn = jnp.where(new_ok, sn, -jnp.inf)
        top = jnp.maximum(jnp.max(sc, axis=1, keepdims=True), jnp.max(sn, axis=1, keepdims=True))
        wc = jnp.exp(sc - top)
        wn = jnp.exp(sn - top)
        total = jnp.sum(wc, axis=1, keepdims=True) + jnp.sum(wn, axis=1, keepdims=True)
        ctx = jnp.dot(wc.astype(jnp.bfloat16), vc_ref[0, :, cols], preferred_element_type=jnp.float32)
        ctx = ctx + jnp.dot(wn.astype(jnp.bfloat16), vn_ref[0, :, cols], preferred_element_type=jnp.float32)
        parts.append((ctx / total).astype(jnp.bfloat16))
    context = jnp.concatenate(parts, axis=1)
    out_ref[0] = jnp.dot(context, wo_ref[...], preferred_element_type=jnp.float32).astype(out_ref.dtype)


def attend_pallas(queries, new_keys, new_values, k_cache, v_cache, w_out, cache_len):
    requests, span, width = k_cache.shape
    new_count = queries.shape[0] // requests
    shape3 = (requests, new_count, width)
    q3, kn3, vn3 = (a.reshape(shape3) for a in (queries, new_keys, new_values))
    new_spec = pl.BlockSpec((1, new_count, width), lambda g, lens: (g, 0, 0))
    cache_spec = pl.BlockSpec((1, span, width), lambda g, lens: (g, 0, 0))
    out = pl.pallas_call(
        attend_kernel,
        out_shape=jax.ShapeDtypeStruct((requests, new_count, w_out.shape[1]), jnp.bfloat16),
        grid_spec=pltpu.PrefetchScalarGridSpec(
            num_scalar_prefetch=1,
            grid=(requests,),
            in_specs=[new_spec, new_spec, new_spec, cache_spec, cache_spec,
                      pl.BlockSpec(w_out.shape, lambda g, lens: (0, 0))],
            out_specs=pl.BlockSpec((1, new_count, w_out.shape[1]), lambda g, lens: (g, 0, 0)),
        ),
    )(cache_len, q3, kn3, vn3, k_cache, v_cache, w_out)
    return out.reshape(queries.shape[0], w_out.shape[1])


def head_view(array, head_size):
    return array.reshape(array.shape[0], array.shape[1] // head_size, head_size)


def attend_padded(queries, new_keys, new_values, cache_keys, cache_values, length):
    head_size = D // HEADS
    new_count = queries.shape[0]
    span = cache_keys.shape[0]
    keys_all = head_view(jnp.concatenate([cache_keys, new_keys], 0), head_size)
    values_all = head_view(jnp.concatenate([cache_values, new_values], 0), head_size)
    query_heads = head_view(queries, head_size)
    scores = jnp.einsum(
        "qhd,khd->hqk", query_heads, keys_all, preferred_element_type=jnp.float32
    ) * head_size ** (-0.5)
    key_pos = jnp.arange(span + new_count, dtype=jnp.int32)[None, :]
    query_pos = jnp.arange(new_count, dtype=jnp.int32)[:, None]
    valid = jnp.where(key_pos < span, key_pos < length, key_pos - span <= query_pos)
    scores = jnp.where(valid[None], scores, -jnp.inf)
    top = jnp.max(scores, axis=-1, keepdims=True)
    weight = jnp.where(valid[None], jnp.exp(scores - top), 0.0)
    total = jnp.sum(weight, axis=-1)
    context = jnp.einsum(
        "hqk,khd->qhd", weight.astype(jnp.bfloat16), values_all, preferred_element_type=jnp.float32
    )
    context = context / jnp.transpose(total)[:, :, None]
    return context.reshape(new_count, queries.shape[1]).astype(jnp.bfloat16)


def attend_all(queries, new_keys, new_values, k_cache, v_cache, cache_len):
    request_count = k_cache.shape[0]
    req_shape = (request_count, queries.shape[0] // request_count, queries.shape[1])
    span = req_shape[1]
    parts = [
        attend_padded(
            queries[g * span:(g + 1) * span],
            new_keys[g * span:(g + 1) * span],
            new_values[g * span:(g + 1) * span],
            k_cache[g],
            v_cache[g],
            cache_len[g],
        )
        for g in range(request_count)
    ]
    return jnp.concatenate(parts, 0)


def project_rows(whole, w_query, w_key, w_value):
    width = w_query.shape[1]
    joined = jnp.concatenate([w_query, w_key, w_value], 1)
    all_three = jnp.dot(whole, joined, preferred_element_type=jnp.float32).astype(jnp.bfloat16)
    return (all_three[:, :width], all_three[:, width:2 * width], all_three[:, 2 * width:])


def finish_rows(partial_sum, local, ln_gain, ln_bias):
    row_count, feat_width = local.shape
    attended = scatter_sum_tp(partial_sum)
    summed = local.astype(jnp.float32) + attended
    first_sum, square_sum = sum_tp(
        jnp.stack([jnp.sum(summed, axis=1), jnp.sum(summed * summed, axis=1)])
    )
    row_mean = first_sum / D
    row_var = square_sum / D - row_mean * row_mean
    offset = lax.axis_index("tp") * feat_width
    gain_part = lax.dynamic_slice_in_dim(ln_gain, offset, feat_width, 0)
    bias_part = lax.dynamic_slice_in_dim(ln_bias, offset, feat_width, 0)
    scaled = (summed - row_mean[:, None]) / jnp.sqrt(row_var[:, None] + 1e-05)
    return (scaled * gain_part + bias_part).astype(jnp.bfloat16)


def shards(
    tokens, placement, cache_len, w_query, w_key, w_value, w_out, k_cache, v_cache, ln_gain, ln_bias
):
    row_count, feat_width = tokens.shape
    block_count = placement.shape[0]
    block_rows = row_count // block_count
    per_peer = block_count // lax.axis_size("req")
    send_slot = placement // block_count * per_peer + placement % per_peer
    choose = (
        send_slot[None, :] == jnp.arange(block_count, dtype=jnp.int32)[:, None]
    ).astype(jnp.bfloat16)

    def to_blocks(array):
        return array.reshape(block_count, block_rows, array.shape[1])

    ordered = jnp.einsum(
        "ja,aif->jif", choose, to_blocks(tokens), preferred_element_type=jnp.float32
    ).astype(jnp.bfloat16)
    arrived = lax.all_to_all(
        ordered, "req", split_axis=0, concat_axis=0, tiled=True
    ).reshape(row_count, feat_width)
    whole = gather_tp(arrived)
    queries, new_keys, new_values = project_rows(whole, w_query, w_key, w_value)
    partial_sum = attend_pallas(queries, new_keys, new_values, k_cache, v_cache, w_out, cache_len)
    normed = finish_rows(partial_sum, arrived, ln_gain, ln_bias)
    returned = lax.all_to_all(to_blocks(normed), "req", split_axis=0, concat_axis=0, tiled=True)
    back = jnp.einsum("ja,jif->aif", choose, returned, preferred_element_type=jnp.float32)
    return back.astype(jnp.bfloat16).reshape(row_count, feat_width)


def solution(mesh):
    in_specs = (
        P("req", "tp"),
        P("req"),
        P("req"),
        P(None, "tp"),
        P(None, "tp"),
        P(None, "tp"),
        P("tp", None),
        P("req", None, "tp"),
        P("req", None, "tp"),
        P(),
        P(),
    )
    out_specs = P("req", "tp")
    return jax.shard_map(shards, mesh=mesh, in_specs=in_specs, out_specs=out_specs, check_vma=False)
```

```python
import jax
import jax.numpy as jnp
from jax import lax
from jax.experimental import pallas as pl
from jax.experimental.pallas import tpu as pltpu
from jax.sharding import PartitionSpec as P

D = 1024
HEADS = 16


def gather_tp(part):
    count = lax.axis_size("tp")
    copies = jnp.broadcast_to(part[None], (count,) + part.shape)
    got = lax.all_to_all(copies, "tp", 0, 0, tiled=True)
    return jnp.moveaxis(got, 0, 1).reshape(part.shape[0], count * part.shape[1])


def scatter_sum_tp(whole):
    count = lax.axis_size("tp")
    rows, width = whole.shape
    pieces = jnp.moveaxis(whole.reshape(rows, count, width // count), 1, 0)
    got = lax.all_to_all(pieces, "tp", 0, 0, tiled=True)
    return jnp.sum(got.astype(jnp.float32), axis=0)


def sum_tp(stats):
    count = lax.axis_size("tp")
    copies = jnp.broadcast_to(stats[None], (count,) + stats.shape)
    got = lax.all_to_all(copies, "tp", 0, 0, tiled=True)
    return jnp.sum(got, axis=0)


HEAD = 64


def attend_kernel(lens_ref, q_ref, kn_ref, vn_ref, kc_ref, vc_ref, out_ref):
    g = pl.program_id(0)
    length = lens_ref[g]
    new_count = q_ref.shape[1]
    span = kc_ref.shape[1]
    heads = q_ref.shape[2] // HEAD
    cache_pos = lax.broadcasted_iota(jnp.int32, (new_count, span), 1)
    cache_ok = cache_pos < length
    row = lax.broadcasted_iota(jnp.int32, (new_count, new_count), 0)
    col = lax.broadcasted_iota(jnp.int32, (new_count, new_count), 1)
    new_ok = col <= row
    dims = (((1,), (1,)), ((), ()))
    for h in range(heads):
        cols = slice(h * HEAD, (h + 1) * HEAD)
        qh = q_ref[0, :, cols]
        sc = lax.dot_general(qh, kc_ref[0, :, cols], dims, preferred_element_type=jnp.float32) * HEAD ** (-0.5)
        sn = lax.dot_general(qh, kn_ref[0, :, cols], dims, preferred_element_type=jnp.float32) * HEAD ** (-0.5)
        sc = jnp.where(cache_ok, sc, -jnp.inf)
        sn = jnp.where(new_ok, sn, -jnp.inf)
        top = jnp.maximum(jnp.max(sc, axis=1, keepdims=True), jnp.max(sn, axis=1, keepdims=True))
        wc = jnp.exp(sc - top)
        wn = jnp.exp(sn - top)
        total = jnp.sum(wc, axis=1, keepdims=True) + jnp.sum(wn, axis=1, keepdims=True)
        ctx = jnp.dot(wc.astype(jnp.bfloat16), vc_ref[0, :, cols], preferred_element_type=jnp.float32)
        ctx = ctx + jnp.dot(wn.astype(jnp.bfloat16), vn_ref[0, :, cols], preferred_element_type=jnp.float32)
        out_ref[0, :, cols] = (ctx / total).astype(out_ref.dtype)


def attend_pallas(joined, k_cache, v_cache, cache_len):
    requests, span, width = k_cache.shape
    new_count = joined.shape[0] // requests
    packed = joined.reshape(requests, new_count, joined.shape[1])

    def new_spec(part):
        return pl.BlockSpec((1, new_count, width), lambda g, lens: (g, 0, part))

    cache_spec = pl.BlockSpec((1, span, width), lambda g, lens: (g, 0, 0))
    out = pl.pallas_call(
        attend_kernel,
        out_shape=jax.ShapeDtypeStruct((requests, new_count, width), jnp.bfloat16),
        grid_spec=pltpu.PrefetchScalarGridSpec(
            num_scalar_prefetch=1,
            grid=(requests,),
            in_specs=[new_spec(0), new_spec(1), new_spec(2), cache_spec, cache_spec],
            out_specs=new_spec(0),
        ),
    )(cache_len, packed, packed, packed, k_cache, v_cache)
    return out.reshape(joined.shape[0], width)


def head_view(array, head_size):
    return array.reshape(array.shape[0], array.shape[1] // head_size, head_size)


def attend_padded(queries, new_keys, new_values, cache_keys, cache_values, length):
    head_size = D // HEADS
    new_count = queries.shape[0]
    span = cache_keys.shape[0]
    keys_all = head_view(jnp.concatenate([cache_keys, new_keys], 0), head_size)
    values_all = head_view(jnp.concatenate([cache_values, new_values], 0), head_size)
    query_heads = head_view(queries, head_size)
    scores = jnp.einsum(
        "qhd,khd->hqk", query_heads, keys_all, preferred_element_type=jnp.float32
    ) * head_size ** (-0.5)
    key_pos = jnp.arange(span + new_count, dtype=jnp.int32)[None, :]
    query_pos = jnp.arange(new_count, dtype=jnp.int32)[:, None]
    valid = jnp.where(key_pos < span, key_pos < length, key_pos - span <= query_pos)
    scores = jnp.where(valid[None], scores, -jnp.inf)
    top = jnp.max(scores, axis=-1, keepdims=True)
    weight = jnp.where(valid[None], jnp.exp(scores - top), 0.0)
    total = jnp.sum(weight, axis=-1)
    context = jnp.einsum(
        "hqk,khd->qhd", weight.astype(jnp.bfloat16), values_all, preferred_element_type=jnp.float32
    )
    context = context / jnp.transpose(total)[:, :, None]
    return context.reshape(new_count, queries.shape[1]).astype(jnp.bfloat16)


def attend_all(queries, new_keys, new_values, k_cache, v_cache, cache_len):
    request_count = k_cache.shape[0]
    req_shape = (request_count, queries.shape[0] // request_count, queries.shape[1])
    span = req_shape[1]
    parts = [
        attend_padded(
            queries[g * span:(g + 1) * span],
            new_keys[g * span:(g + 1) * span],
            new_values[g * span:(g + 1) * span],
            k_cache[g],
            v_cache[g],
            cache_len[g],
        )
        for g in range(request_count)
    ]
    return jnp.concatenate(parts, 0)


def project_rows(whole, w_query, w_key, w_value):
    width = w_query.shape[1]
    joined = jnp.concatenate([w_query, w_key, w_value], 1)
    all_three = jnp.dot(whole, joined, preferred_element_type=jnp.float32).astype(jnp.bfloat16)
    return all_three


def finish_rows(context, local, w_out, ln_gain, ln_bias):
    row_count, feat_width = local.shape
    partial_sum = jnp.dot(context, w_out, preferred_element_type=jnp.float32)
    attended = scatter_sum_tp(partial_sum.astype(jnp.bfloat16))
    summed = local.astype(jnp.float32) + attended
    first_sum, square_sum = sum_tp(
        jnp.stack([jnp.sum(summed, axis=1), jnp.sum(summed * summed, axis=1)])
    )
    row_mean = first_sum / D
    row_var = square_sum / D - row_mean * row_mean
    offset = lax.axis_index("tp") * feat_width
    gain_part = lax.dynamic_slice_in_dim(ln_gain, offset, feat_width, 0)
    bias_part = lax.dynamic_slice_in_dim(ln_bias, offset, feat_width, 0)
    scaled = (summed - row_mean[:, None]) / jnp.sqrt(row_var[:, None] + 1e-05)
    return (scaled * gain_part + bias_part).astype(jnp.bfloat16)


def shards(
    tokens, placement, cache_len, w_query, w_key, w_value, w_out, k_cache, v_cache, ln_gain, ln_bias
):
    row_count, feat_width = tokens.shape
    block_count = placement.shape[0]
    block_rows = row_count // block_count
    per_peer = block_count // lax.axis_size("req")
    send_slot = placement // block_count * per_peer + placement % per_peer
    choose = (
        send_slot[None, :] == jnp.arange(block_count, dtype=jnp.int32)[:, None]
    ).astype(jnp.bfloat16)

    def to_blocks(array):
        return array.reshape(block_count, block_rows, array.shape[1])

    ordered = jnp.einsum(
        "ja,aif->jif", choose, to_blocks(tokens), preferred_element_type=jnp.float32
    ).astype(jnp.bfloat16)
    arrived = lax.all_to_all(
        ordered, "req", split_axis=0, concat_axis=0, tiled=True
    ).reshape(row_count, feat_width)
    whole = gather_tp(arrived)
    joined = project_rows(whole, w_query, w_key, w_value)
    context = attend_pallas(joined, k_cache, v_cache, cache_len)
    normed = finish_rows(context, arrived, w_out, ln_gain, ln_bias)
    returned = lax.all_to_all(to_blocks(normed), "req", split_axis=0, concat_axis=0, tiled=True)
    back = jnp.einsum("ja,jif->aif", choose, returned, preferred_element_type=jnp.float32)
    return back.astype(jnp.bfloat16).reshape(row_count, feat_width)


def solution(mesh):
    in_specs = (
        P("req", "tp"),
        P("req"),
        P("req"),
        P(None, "tp"),
        P(None, "tp"),
        P(None, "tp"),
        P("tp", None),
        P("req", None, "tp"),
        P("req", None, "tp"),
        P(),
        P(),
    )
    out_specs = P("req", "tp")
    return jax.shard_map(shards, mesh=mesh, in_specs=in_specs, out_specs=out_specs, check_vma=False)
```
